32 devices in a mesh: groups: 1, orb: 32 (over z, y, x, core), aux: 1.
Axes of the slice: x: 2, y: 2, z: 4, core: 2. Of those that a mesh axis runs over, the one named last changes fastest.
Arguments:
- exchange_integral_halves: float32 [1, 128, 256, 256], P('aux', ('groups', 'orb')), may hold values from -3 to 3
- amplitudes: bfloat16 [128, 256, 256], P(('groups', 'orb')), may hold values from -6 to 6
- pair_slot_orbitals: int32 [128, 2], P('groups'), may hold values from 0 to 63
- pao_domain: int32 [64, 256], P('groups'), may hold values from 0 to 511, as said below
- pao_intersection: bfloat16 [512, 512], P('groups'), as said below
- pao_fock: bfloat16 [512, 512], P('groups'), as said below
- occ_energy: float32 [64], P('groups'), may hold values from -1.5 to -0.3
- coupled_pair_owner: int32 [128, 8], P(('groups', 'orb')), may hold values from 0 to 31, all different within a row; in each aligned block of 4 rows (0 to 3, 4 to 7, ...) at most 2 rows name the same one
- coupled_pair_slot: int32 [128, 8], P(('groups', 'orb')), may hold values from 0 to 3
- coupling_swap_flag: int32 [128, 8], P(('groups', 'orb')), may hold values from 0 to 1
- coupling_fock_element: float32 [128, 8], P(('groups', 'orb')), may hold values from -1.2 to 1.2
Outputs:
- residual: float32 [128, 256, 256], P(('groups', 'orb'), 'aux')
- updated_pair_amplitudes: bfloat16 [128, 256, 256], P(('groups', 'orb'), 'aux')
The draws below stay inside these ranges and needn't reach their ends.
Inputs may be any that keep to these rules, and one draw needn't show every extreme that they name: `pao_domain`: each orbital's 256 domain entries are distinct. `coupled_pair_owner`: the 8 owners in one row differ; among the 4 pair slots of one owner no owner is named by more than 2 rows, a bound that some block reaches. `pao_intersection`: symmetric with unit diagonal. `pao_fock`: symmetric with diagonal from 0.5 to 3.
All inputs are finite; a program needn't handle non-finite values.
Results may differ from the reference program's by a relative error of at most 0.012.
Values may be sent and summed in bfloat16 or wider, within the bound.
No kernel may reach another device: no remote copies, remote signals or barrier semaphores. Data moves between devices by JAX's collectives and lax.ppermute only.
A program may use at most 128 MiB of HBM per device.

```python
import math
import jax
import jax.numpy as jnp
import numpy as np
from jax import lax

DOMAIN_WIDTH = 256
PAOS = 512
COUPLING_TOTAL = 8
SLOTS_PER_OWNER = 4
SLOT_TOTAL = 128
ORBITAL_COUNT = 64
MAX_SOURCE_SLOTS = 2
N_ORB = 32
N_AUX = 1


def draw_pao_domain(key, part):
    scores = jax.random.randint(key, (ORBITAL_COUNT, PAOS), 0, 1 << 20) * PAOS + jnp.arange(PAOS, dtype=jnp.int32)[None, :]
    picked = lax.top_k(scores, DOMAIN_WIDTH)[1]
    return picked.astype(jnp.int32)


def draw_pao_intersection(key, part):
    raw = jax.random.normal(key, (PAOS, PAOS), jnp.float32)
    symmetric = (raw + raw.T) * 0.03
    identity = jnp.eye(PAOS, dtype=jnp.float32)
    return (symmetric * (1.0 - identity) + identity).astype(jnp.bfloat16)


def draw_pao_fock(key, part):
    diag_key = jax.random.fold_in(key, 7)
    raw = jax.random.normal(key, (PAOS, PAOS), jnp.float32)
    diagonal = jax.random.uniform(diag_key, (PAOS,), jnp.float32, 0.5, 3.0)
    symmetric = (raw + raw.T) * 0.02
    identity = jnp.eye(PAOS, dtype=jnp.float32)
    return (symmetric * (1.0 - identity) + identity * diagonal[None, :]).astype(jnp.bfloat16)


def plant(drawn, own_key, smallest, top_value):
    dims = drawn.shape
    spot = [jax.random.randint(jax.random.fold_in(own_key, axis), (), 0, dims[axis]) for axis in range(len(dims))]
    drawn = drawn.at[tuple(spot)].set(smallest)
    longest = dims.index(max(dims))
    spot[longest] = (spot[longest] + 1) % dims[longest]
    return drawn.at[tuple(spot)].set(top_value)


def steps_of(key, extent, pieces, low, top_value):
    level = 1.0
    for axis_at, parts in pieces:
        draws = jax.random.uniform(jax.random.fold_in(jax.random.fold_in(key, 6), axis_at), (parts,), jnp.float32, low / len(pieces), top_value / len(pieces))
        level = level * jnp.repeat(jnp.exp(draws), extent[axis_at] // parts).reshape((-1,) + (1,) * (len(extent) - 1 - axis_at))
    return level


def shared_out(key, own, number, rows, count, top, bound, slope):
    sequence = jax.random.permutation(key, count)
    packed, ordinary = load_shares(count, rows * top, bound, slope, True), load_shares(count, rows * top, bound, slope, False)
    places = jnp.arange(count)

    def named(sizes, turn):
        used = int((sizes > 0).sum())
        fixed = max(1, used // 4)
        moved = fixed + (places - fixed + turn * (used - fixed)) % max(1, count - fixed)
        return jnp.zeros((count,), jnp.int32).at[sequence[jnp.where(places < fixed, places, moved)]].set(jnp.asarray(sizes, jnp.int32))

    sizes = jnp.where(number % 4 == 0, named(packed, number // 4), named(ordinary, number - number // 4 - 1))
    mixed = jax.random.permutation(jax.random.fold_in(own, 3), count)
    giver, sink = mixed[0:count // 2 * 2:2], mixed[1:count // 2 * 2:2]
    margin = jnp.minimum(sizes[giver] - 1, bound - sizes[sink]) // 2
    margin = jnp.where((giver == sequence[0]) | (sink == sequence[0]) | (sizes[sink] == 0), 0, jnp.maximum(margin, 0))
    moved = jax.random.randint(jax.random.fold_in(own, 4), (count // 2,), 0, 1 << 20) % (margin + 1)
    sizes = sizes.at[giver].add(-moved).at[sink].add(moved)
    items = jnp.searchsorted(jnp.cumsum(sizes), jnp.arange(rows * top), side="right").astype(jnp.int32)
    listing = items.reshape(top, rows).T
    listing = listing[jax.random.permutation(jax.random.fold_in(own, 1), rows)]
    turn = jax.random.randint(jax.random.fold_in(own, 2), (rows, 1), 0, top)
    return jnp.take_along_axis(listing, (jnp.arange(top)[None, :] + turn) % top, axis=1)


def load_shares(count, total, limit, slope, full):
    portions = [(1 << 20) // math.isqrt(grade ** slope) + 1 for grade in range(1, count + 1)]
    largest = limit if full else min(limit, max(-(-total // count), total * portions[0] // sum(portions)))
    least = 1 if total - largest >= count - 1 else 0
    given, surplus = [largest] + [least] * (count - 1), total - largest - least * (count - 1)
    while surplus > 0:
        free = [i for i in range(1, count) if given[i] < largest] or [i for i in range(1, count) if given[i] < limit]
        whole, left = sum([portions[i] for i in free]), surplus
        for i in free:
            extra = min(limit - given[i], max(1, left * portions[i] // whole), surplus)
            given[i] = given[i] + extra
            surplus = surplus - extra
    return np.array(given)


def normal_values(key, extent, deviation, bound, split=(), kind=jnp.bfloat16):
    result = deviation * jax.random.normal(key, extent, jnp.float32)
    if split:
        result = result * steps_of(key, extent, split, -0.22, 0.18)
    return jnp.clip(result, -bound, bound).astype(kind)


def setup_inputs(seed: int = 0, part: int = 0) -> dict:
    splits = jax.random.split(jax.random.key(seed), 12)
    part_keys = jax.random.split(jax.random.fold_in(splits[11], part), 12)
    exchange_integral_halves = normal_values(part_keys[0], (N_AUX, SLOT_TOTAL, DOMAIN_WIDTH, DOMAIN_WIDTH), 0.5, 3.0, ((1, 32),), jnp.float32)
    amplitudes = normal_values(part_keys[1], (SLOT_TOTAL, DOMAIN_WIDTH, DOMAIN_WIDTH), 1.0, 6.0, ((0, 32),))
    pair_slot_orbitals = plant(jax.random.randint(part_keys[2], (SLOT_TOTAL, 2), 0, ORBITAL_COUNT), jax.random.fold_in(part_keys[2], 1), 0, ORBITAL_COUNT - 1).astype(jnp.int32)
    pao_domain = draw_pao_domain(jax.random.fold_in(jax.random.fold_in(splits[11], part), 71), part)
    pao_intersection = draw_pao_intersection(jax.random.fold_in(jax.random.fold_in(splits[11], part), 71), part)
    pao_fock = draw_pao_fock(jax.random.fold_in(jax.random.fold_in(splits[11], part), 71), part)
    occ_energy = jnp.clip(jax.random.uniform(part_keys[6], (ORBITAL_COUNT,), jnp.float32, -1.5, -0.3), -1.5, -0.3)
    coupled_pair_owner_keys = jax.random.split(jax.random.fold_in(part_keys[7], 1), SLOT_TOTAL // SLOTS_PER_OWNER)
    coupled_pair_owner_turns = jax.random.permutation(jax.random.fold_in(part_keys[7], 3), SLOT_TOTAL // SLOTS_PER_OWNER)
    coupled_pair_owner = jax.vmap(lambda own, number: shared_out(jax.random.fold_in(part_keys[7], 2), own, number, SLOTS_PER_OWNER, N_ORB, COUPLING_TOTAL, MAX_SOURCE_SLOTS, 2))(coupled_pair_owner_keys, coupled_pair_owner_turns).reshape((SLOT_TOTAL, COUPLING_TOTAL))
    coupled_pair_slot = plant(jax.random.randint(part_keys[8], (SLOT_TOTAL, COUPLING_TOTAL), 0, SLOTS_PER_OWNER), jax.random.fold_in(part_keys[8], 1), 0, SLOTS_PER_OWNER - 1).astype(jnp.int32)
    coupling_swap_flag = plant(jax.random.randint(part_keys[9], (SLOT_TOTAL, COUPLING_TOTAL), 0, 2), jax.random.fold_in(part_keys[9], 1), 0, 1).astype(jnp.int32)
    coupling_fock_element = normal_values(part_keys[10], (SLOT_TOTAL, COUPLING_TOTAL), 0.2, 1.2, ((0, 32),), jnp.float32)
    return dict(exchange_integral_halves=exchange_integral_halves, amplitudes=amplitudes, pair_slot_orbitals=pair_slot_orbitals, pao_domain=pao_domain, pao_intersection=pao_intersection, pao_fock=pao_fock, occ_energy=occ_energy, coupled_pair_owner=coupled_pair_owner, coupled_pair_slot=coupled_pair_slot, coupling_swap_flag=coupling_swap_flag, coupling_fock_element=coupling_fock_element)


def submatrix(matrix, rows_ids, cols_ids):
    return jnp.take(jnp.take(matrix, rows_ids, axis=0), cols_ids, axis=1)


def product(left, right):
    return jnp.dot(left.astype(jnp.float32), right.astype(jnp.float32), preferred_element_type=jnp.float32)


def reference(exchange_integral_halves, amplitudes, pair_slot_orbitals, pao_domain, pao_intersection, pao_fock, occ_energy, coupled_pair_owner, coupled_pair_slot, coupling_swap_flag, coupling_fock_element):
    pao_energy = jnp.diagonal(pao_fock).astype(jnp.float32)

    def single_pair_residual(slot_id):
        orb_i = pair_slot_orbitals[slot_id, 0]
        orb_j = pair_slot_orbitals[slot_id, 1]
        dom_i = pao_domain[orb_i]
        dom_j = pao_domain[orb_j]
        pair_amp = amplitudes[slot_id]
        left_f = product(submatrix(pao_fock, dom_i, dom_i), pair_amp).astype(jnp.bfloat16)
        left_s = product(submatrix(pao_intersection, dom_i, dom_i), pair_amp).astype(jnp.bfloat16)
        s_right = submatrix(pao_intersection, dom_j, dom_j)
        f_right = submatrix(pao_fock, dom_j, dom_j)
        energy_sum = occ_energy[orb_i] + occ_energy[orb_j]
        summed = jnp.sum(exchange_integral_halves[:, slot_id], axis=0)
        summed = summed + product(left_f, s_right)
        summed = summed + product(left_s, f_right)
        summed = summed - energy_sum * product(left_s, s_right)

        def couple(column, running):
            global_slot = (coupled_pair_owner[slot_id, column] * SLOTS_PER_OWNER + coupled_pair_slot[slot_id, column]).astype(jnp.int32)
            flipped = coupling_swap_flag[slot_id, column] == 1
            amp_block = amplitudes[global_slot]
            amp_block = jnp.where(flipped, amp_block.T, amp_block)
            first_orb = pair_slot_orbitals[global_slot, 0]
            second_orb = pair_slot_orbitals[global_slot, 1]
            orb_row = jnp.where(flipped, second_orb, first_orb)
            orb_col = jnp.where(flipped, first_orb, second_orb)
            reach = product(submatrix(pao_intersection, dom_i, pao_domain[orb_row]), amp_block).astype(jnp.bfloat16)
            right_map = submatrix(pao_intersection, pao_domain[orb_col], dom_j)
            return running - coupling_fock_element[slot_id, column] * product(reach, right_map)

        summed = lax.fori_loop(0, COUPLING_TOTAL, couple, summed)
        denom = pao_energy[dom_i][:, None] + pao_energy[dom_j][None, :] - energy_sum
        updated = (pair_amp.astype(jnp.float32) - summed / denom).astype(jnp.bfloat16)
        return summed, updated

    residual, updated_pair_amplitudes = lax.map(single_pair_residual, jnp.arange(SLOT_TOTAL, dtype=jnp.int32))
    return residual, updated_pair_amplitudes
```

```python
import jax
import jax.numpy as jnp
from jax import lax
from jax.sharding import PartitionSpec as P


def one_hot(ids, width):
    return (ids[..., None] == jnp.arange(width, dtype=ids.dtype)).astype(jnp.bfloat16)


def sel_rows(onehot, matrix):
    return jnp.einsum(
        "...rk,kc->...rc", onehot, matrix, preferred_element_type=jnp.float32
    ).astype(jnp.bfloat16)


def shards(
    exchange_integral_halves,
    amplitudes,
    pair_slot_orbitals,
    pao_domain,
    pao_intersection,
    pao_fock,
    occ_energy,
    coupled_pair_owner,
    coupled_pair_slot,
    coupling_swap_flag,
    coupling_fock_element,
):
    slot_count, extent = amplitudes.shape[0], amplitudes.shape[1]
    paos = pao_intersection.shape[0]
    halves = lax.axis_size("aux")
    owner_index = lax.axis_index("orb")
    aux_index = lax.axis_index("aux")
    half_rows = extent // halves
    row_first = aux_index * half_rows

    every_amp = lax.all_gather(amplitudes, "orb", axis=0, tiled=True)

    own_slots = owner_index * slot_count + jnp.arange(slot_count, dtype=jnp.int32)
    orb_i = pair_slot_orbitals[own_slots, 0]
    orb_j = pair_slot_orbitals[own_slots, 1]
    dom_i = pao_domain[orb_i]
    dom_j = pao_domain[orb_j]
    rows_dom = lax.dynamic_slice_in_dim(dom_i, row_first, half_rows, 1)
    energy_sum = occ_energy[orb_i] + occ_energy[orb_j]

    global_slot = coupled_pair_owner * slot_count + coupled_pair_slot
    flipped = coupling_swap_flag == 1
    first_orb = pair_slot_orbitals[global_slot, 0]
    second_orb = pair_slot_orbitals[global_slot, 1]
    orb_p = jnp.where(flipped, second_orb, first_orb)
    orb_q = jnp.where(flipped, first_orb, second_orb)

    oh_rows = one_hot(rows_dom, paos)
    oh_i = one_hot(dom_i, paos)
    oh_j = one_hot(dom_j, paos)
    oh_p = one_hot(pao_domain[orb_p], paos)
    oh_q = one_hot(pao_domain[orb_q], paos)

    rs = sel_rows(oh_rows, pao_intersection)
    rf = sel_rows(oh_rows, pao_fock)
    s_ii = jnp.einsum("brk,bak->bra", rs, oh_i, preferred_element_type=jnp.float32).astype(jnp.bfloat16)
    f_ii = jnp.einsum("brk,bak->bra", rf, oh_i, preferred_element_type=jnp.float32).astype(jnp.bfloat16)
    js = sel_rows(oh_j, pao_intersection)
    jf = sel_rows(oh_j, pao_fock)
    s_jj = jnp.einsum("bjk,bak->bja", js, oh_j, preferred_element_type=jnp.float32).astype(jnp.bfloat16)
    f_jj = jnp.einsum("bjk,bak->bja", jf, oh_j, preferred_element_type=jnp.float32).astype(jnp.bfloat16)
    col_s = jnp.einsum("kc,bjc->bkj", pao_intersection, oh_j, preferred_element_type=jnp.float32).astype(
        jnp.bfloat16
    )
    s_ip = jnp.einsum("brk,bcpk->bcrp", rs, oh_p, preferred_element_type=jnp.float32).astype(jnp.bfloat16)
    s_qj = jnp.einsum("bcqk,bkj->bcqj", oh_q, col_s, preferred_element_type=jnp.float32).astype(jnp.bfloat16)

    summed = lax.psum_scatter(
        exchange_integral_halves[0], "aux", scatter_dimension=1, tiled=True
    )
    left_f = jnp.einsum("bra,bad->brd", f_ii, amplitudes, preferred_element_type=jnp.float32).astype(
        jnp.bfloat16
    )
    left_s = jnp.einsum("bra,bad->brd", s_ii, amplitudes, preferred_element_type=jnp.float32).astype(
        jnp.bfloat16
    )
    summed = summed + jnp.einsum("brd,bdj->brj", left_f, s_jj, preferred_element_type=jnp.float32)
    summed = summed + jnp.einsum("brd,bdj->brj", left_s, f_jj, preferred_element_type=jnp.float32)
    summed = summed - energy_sum[:, None, None] * jnp.einsum(
        "brd,bdj->brj", left_s, s_jj, preferred_element_type=jnp.float32
    )

    blocks = every_amp[global_slot]
    blocks = jnp.where(flipped[:, :, None, None], jnp.swapaxes(blocks, 2, 3), blocks)
    reach = jnp.einsum("bcrp,bcpd->bcrd", s_ip, blocks, preferred_element_type=jnp.float32).astype(
        jnp.bfloat16
    )
    for column in range(coupled_pair_owner.shape[1]):
        summed = summed - coupling_fock_element[:, column][:, None, None] * jnp.einsum(
            "brd,bdj->brj", reach[:, column], s_qj[:, column], preferred_element_type=jnp.float32
        )

    pao_energy = jnp.diagonal(pao_fock).astype(jnp.float32)
    denom = (
        pao_energy[rows_dom][:, :, None] + pao_energy[dom_j][:, None, :] - energy_sum[:, None, None]
    )
    amp_rows = lax.dynamic_slice_in_dim(amplitudes, row_first, half_rows, 1).astype(jnp.float32)
    updated = (amp_rows - summed / denom).astype(jnp.bfloat16)
    return (summed, updated)


def solution(mesh):
    placed = (
        P("aux", ("groups", "orb"), None, None),
        P(("groups", "orb"), None, None),
        P("groups", None),
        P("groups", None),
        P("groups", None),
        P("groups", None),
        P("groups"),
        P(("groups", "orb"), None),
        P(("groups", "orb"), None),
        P(("groups", "orb"), None),
        P(("groups", "orb"), None),
    )
    return jax.shard_map(
        shards,
        mesh=mesh,
        in_specs=placed,
        out_specs=(P(("groups", "orb"), "aux", None), P(("groups", "orb"), "aux", None)),
        check_vma=False,
    )
```

```python
import jax
import jax.numpy as jnp
from jax import lax
from jax.sharding import PartitionSpec as P


def one_hot(ids, width):
    return (ids[..., None] == jnp.arange(width, dtype=ids.dtype)).astype(jnp.bfloat16)


def sel_rows(onehot, matrix):
    return jnp.einsum(
        "...rk,kc->...rc", onehot, matrix, preferred_element_type=jnp.float32
    ).astype(jnp.bfloat16)


def shards(
    exchange_integral_halves,
    amplitudes,
    pair_slot_orbitals,
    pao_domain,
    pao_intersection,
    pao_fock,
    occ_energy,
    coupled_pair_owner,
    coupled_pair_slot,
    coupling_swap_flag,
    coupling_fock_element,
):
    slot_count, extent = amplitudes.shape[0], amplitudes.shape[1]
    paos = pao_intersection.shape[0]
    halves = lax.axis_size("aux")
    owner_index = lax.axis_index("orb_hi") * 2 + lax.axis_index("orb_lo")
    aux_index = lax.axis_index("aux")
    half_rows = extent // halves
    row_first = aux_index * half_rows

    pair_index = lax.axis_index("orb_lo")
    mine = lax.all_gather(amplitudes, "orb_hi", axis=0, tiled=True)
    other = lax.ppermute(mine, "orb_lo", perm=[(0, 1), (1, 0)])

    own_slots = owner_index * slot_count + jnp.arange(slot_count, dtype=jnp.int32)
    orb_i = pair_slot_orbitals[own_slots, 0]
    orb_j = pair_slot_orbitals[own_slots, 1]
    dom_i = pao_domain[orb_i]
    dom_j = pao_domain[orb_j]
    rows_dom = lax.dynamic_slice_in_dim(dom_i, row_first, half_rows, 1)
    energy_sum = occ_energy[orb_i] + occ_energy[orb_j]

    global_slot = coupled_pair_owner * slot_count + coupled_pair_slot
    flipped = coupling_swap_flag == 1
    first_orb = pair_slot_orbitals[global_slot, 0]
    second_orb = pair_slot_orbitals[global_slot, 1]
    orb_p = jnp.where(flipped, second_orb, first_orb)
    orb_q = jnp.where(flipped, first_orb, second_orb)

    oh_rows = one_hot(rows_dom, paos)
    oh_i = one_hot(dom_i, paos)
    oh_j = one_hot(dom_j, paos)
    oh_p = one_hot(pao_domain[orb_p], paos)
    oh_q = one_hot(pao_domain[orb_q], paos)

    rs = sel_rows(oh_rows, pao_intersection)
    rf = sel_rows(oh_rows, pao_fock)
    s_ii = jnp.einsum("brk,bak->bra", rs, oh_i, preferred_element_type=jnp.float32).astype(jnp.bfloat16)
    f_ii = jnp.einsum("brk,bak->bra", rf, oh_i, preferred_element_type=jnp.float32).astype(jnp.bfloat16)
    js = sel_rows(oh_j, pao_intersection)
    jf = sel_rows(oh_j, pao_fock)
    s_jj = jnp.einsum("bjk,bak->bja", js, oh_j, preferred_element_type=jnp.float32).astype(jnp.bfloat16)
    f_jj = jnp.einsum("bjk,bak->bja", jf, oh_j, preferred_element_type=jnp.float32).astype(jnp.bfloat16)
    col_s = jnp.einsum("kc,bjc->bkj", pao_intersection, oh_j, preferred_element_type=jnp.float32).astype(
        jnp.bfloat16
    )
    s_ip = jnp.einsum("brk,bcpk->bcrp", rs, oh_p, preferred_element_type=jnp.float32).astype(jnp.bfloat16)
    s_qj = jnp.einsum("bcqk,bkj->bcqj", oh_q, col_s, preferred_element_type=jnp.float32).astype(jnp.bfloat16)

    summed = lax.psum_scatter(
        exchange_integral_halves[0], "aux", scatter_dimension=1, tiled=True
    )
    left_f = jnp.einsum("bra,bad->brd", f_ii, amplitudes, preferred_element_type=jnp.float32).astype(
        jnp.bfloat16
    )
    left_s = jnp.einsum("bra,bad->brd", s_ii, amplitudes, preferred_element_type=jnp.float32).astype(
        jnp.bfloat16
    )
    summed = summed + jnp.einsum("brd,bdj->brj", left_f, s_jj, preferred_element_type=jnp.float32)
    summed = summed + jnp.einsum("brd,bdj->brj", left_s, f_jj, preferred_element_type=jnp.float32)
    summed = summed - energy_sum[:, None, None] * jnp.einsum(
        "brd,bdj->brj", left_s, s_jj, preferred_element_type=jnp.float32
    )

    local_slot = (coupled_pair_owner // 2) * slot_count + coupled_pair_slot
    same_side = (coupled_pair_owner % 2) == pair_index
    blocks = jnp.where(same_side[:, :, None, None], mine[local_slot], other[local_slot])
    blocks = jnp.where(flipped[:, :, None, None], jnp.swapaxes(blocks, 2, 3), blocks)
    reach = jnp.einsum("bcrp,bcpd->bcrd", s_ip, blocks, preferred_element_type=jnp.float32).astype(
        jnp.bfloat16
    )
    for column in range(coupled_pair_owner.shape[1]):
        summed = summed - coupling_fock_element[:, column][:, None, None] * jnp.einsum(
            "brd,bdj->brj", reach[:, column], s_qj[:, column], preferred_element_type=jnp.float32
        )

    pao_energy = jnp.diagonal(pao_fock).astype(jnp.float32)
    denom = (
        pao_energy[rows_dom][:, :, None] + pao_energy[dom_j][:, None, :] - energy_sum[:, None, None]
    )
    amp_rows = lax.dynamic_slice_in_dim(amplitudes, row_first, half_rows, 1).astype(jnp.float32)
    updated = (amp_rows - summed / denom).astype(jnp.bfloat16)
    return (summed, updated)


def solution(mesh):
    sizes = dict(mesh.shape)
    split = jax.sharding.Mesh(
        mesh.devices.reshape(sizes["groups"], sizes["orb"] // 2, 2, sizes["aux"]),
        ("groups", "orb_hi", "orb_lo", "aux"),
    )
    owner = ("groups", "orb_hi", "orb_lo")
    placed = (
        P("aux", owner, None, None),
        P(owner, None, None),
        P("groups", None),
        P("groups", None),
        P("groups", None),
        P("groups", None),
        P("groups"),
        P(owner, None),
        P(owner, None),
        P(owner, None),
        P(owner, None),
    )
    return jax.shard_map(
        shards,
        mesh=split,
        in_specs=placed,
        out_specs=(P(owner, "aux", None), P(owner, "aux", None)),
        check_vma=False,
    )
```

```python
import jax
import jax.numpy as jnp
from jax import lax
from jax.experimental import pallas as pl
from jax.experimental.pallas import tpu as pltpu
from jax.sharding import PartitionSpec as P


def one_hot(ids, width):
    return (ids[..., None] == jnp.arange(width, dtype=ids.dtype)).astype(jnp.bfloat16)


def sel_rows(onehot, matrix):
    return jnp.einsum(
        "...rk,kc->...rc", onehot, matrix, preferred_element_type=jnp.float32
    ).astype(jnp.bfloat16)


def coupling_kernel(
    slot_ref, flip_ref, fock_ref, blk_ref, sip_ref, sqj_ref, own_ref, den_ref, amp_ref, res_ref, upd_ref, reach
):
    b, c = pl.program_id(0), pl.program_id(1)
    couplings = pl.num_programs(1)
    at = b * couplings + c

    @pl.when(c == 0)
    def _():
        res_ref[...] = own_ref[...]

    @pl.when(flip_ref[at] == 1)
    def _():
        reach[...] = lax.dot_general(
            sip_ref[...], blk_ref[...], (((1,), (1,)), ((), ())), preferred_element_type=jnp.float32
        ).astype(jnp.bfloat16)

    @pl.when(flip_ref[at] != 1)
    def _():
        reach[...] = jnp.dot(sip_ref[...], blk_ref[...], preferred_element_type=jnp.float32).astype(
            jnp.bfloat16
        )

    res_ref[...] = res_ref[...] - fock_ref[at] * jnp.dot(
        reach[...], sqj_ref[...], preferred_element_type=jnp.float32
    )

    @pl.when(c == couplings - 1)
    def _():
        upd_ref[...] = (amp_ref[...].astype(jnp.float32) - res_ref[...] / den_ref[...]).astype(jnp.bfloat16)


def couple_and_update(every_amp, global_slot, flipped, fock, s_ip, s_qj, own, denom, amp_rows):
    slots, couplings = global_slot.shape
    rows, cols = own.shape[1], own.shape[2]
    extent = every_amp.shape[1]
    grid_spec = pltpu.PrefetchScalarGridSpec(
        num_scalar_prefetch=3,
        grid=(slots, couplings),
        in_specs=[
            pl.BlockSpec((None, extent, extent), lambda b, c, gs, fl, fe: (gs[b * couplings + c], 0, 0)),
            pl.BlockSpec((None, None, rows, extent), lambda b, c, gs, fl, fe: (b, c, 0, 0)),
            pl.BlockSpec((None, None, extent, cols), lambda b, c, gs, fl, fe: (b, c, 0, 0)),
            pl.BlockSpec((None, rows, cols), lambda b, c, gs, fl, fe: (b, 0, 0)),
            pl.BlockSpec((None, rows, cols), lambda b, c, gs, fl, fe: (b, 0, 0)),
            pl.BlockSpec((None, rows, cols), lambda b, c, gs, fl, fe: (b, 0, 0)),
        ],
        out_specs=[
            pl.BlockSpec((None, rows, cols), lambda b, c, gs, fl, fe: (b, 0, 0)),
            pl.BlockSpec((None, rows, cols), lambda b, c, gs, fl, fe: (b, 0, 0)),
        ],
        scratch_shapes=[pltpu.VMEM((rows, extent), jnp.bfloat16)],
    )
    flops = 4 * slots * couplings * rows * extent * extent
    moved = slots * couplings * (extent * extent * 2 + rows * extent * 2 + extent * cols * 2) + slots * rows * cols * 18
    return pl.pallas_call(
        coupling_kernel,
        grid_spec=grid_spec,
        out_shape=[
            jax.ShapeDtypeStruct(own.shape, jnp.float32),
            jax.ShapeDtypeStruct(own.shape, jnp.bfloat16),
        ],
        compiler_params=pltpu.CompilerParams(dimension_semantics=("arbitrary", "arbitrary")),
        cost_estimate=pl.CostEstimate(flops=flops, bytes_accessed=moved, transcendentals=0),
    )(
        global_slot.reshape(-1),
        flipped.astype(jnp.int32).reshape(-1),
        fock.reshape(-1),
        every_amp,
        s_ip,
        s_qj,
        own,
        denom,
        amp_rows,
    )


def shards(
    exchange_integral_halves,
    amplitudes,
    pair_slot_orbitals,
    pao_domain,
    pao_intersection,
    pao_fock,
    occ_energy,
    coupled_pair_owner,
    coupled_pair_slot,
    coupling_swap_flag,
    coupling_fock_element,
):
    slot_count, extent = amplitudes.shape[0], amplitudes.shape[1]
    paos = pao_intersection.shape[0]
    halves = lax.axis_size("aux")
    owner_index = lax.axis_index("orb")
    aux_index = lax.axis_index("aux")
    half_rows = extent // halves
    row_first = aux_index * half_rows

    every_amp = lax.all_gather(amplitudes, "orb", axis=0, tiled=True)

    own_slots = owner_index * slot_count + jnp.arange(slot_count, dtype=jnp.int32)
    orb_i = pair_slot_orbitals[own_slots, 0]
    orb_j = pair_slot_orbitals[own_slots, 1]
    dom_i = pao_domain[orb_i]
    dom_j = pao_domain[orb_j]
    rows_dom = lax.dynamic_slice_in_dim(dom_i, row_first, half_rows, 1)
    energy_sum = occ_energy[orb_i] + occ_energy[orb_j]

    global_slot = coupled_pair_owner * slot_count + coupled_pair_slot
    flipped = coupling_swap_flag == 1
    first_orb = pair_slot_orbitals[global_slot, 0]
    second_orb = pair_slot_orbitals[global_slot, 1]
    orb_p = jnp.where(flipped, second_orb, first_orb)
    orb_q = jnp.where(flipped, first_orb, second_orb)

    oh_rows = one_hot(rows_dom, paos)
    oh_i = one_hot(dom_i, paos)
    oh_j = one_hot(dom_j, paos)
    oh_p = one_hot(pao_domain[orb_p], paos)
    oh_q = one_hot(pao_domain[orb_q], paos)

    rs = sel_rows(oh_rows, pao_intersection)
    rf = sel_rows(oh_rows, pao_fock)
    s_ii = jnp.einsum("brk,bak->bra", rs, oh_i, preferred_element_type=jnp.float32).astype(jnp.bfloat16)
    f_ii = jnp.einsum("brk,bak->bra", rf, oh_i, preferred_element_type=jnp.float32).astype(jnp.bfloat16)
    js = sel_rows(oh_j, pao_intersection)
    jf = sel_rows(oh_j, pao_fock)
    s_jj = jnp.einsum("bjk,bak->bja", js, oh_j, preferred_element_type=jnp.float32).astype(jnp.bfloat16)
    f_jj = jnp.einsum("bjk,bak->bja", jf, oh_j, preferred_element_type=jnp.float32).astype(jnp.bfloat16)
    col_s = jnp.einsum("kc,bjc->bkj", pao_intersection, oh_j, preferred_element_type=jnp.float32).astype(
        jnp.bfloat16
    )
    s_ip = jnp.einsum("brk,bcpk->bcrp", rs, oh_p, preferred_element_type=jnp.float32).astype(jnp.bfloat16)
    s_qj = jnp.einsum("bcqk,bkj->bcqj", oh_q, col_s, preferred_element_type=jnp.float32).astype(jnp.bfloat16)

    summed = lax.psum_scatter(
        exchange_integral_halves[0], "aux", scatter_dimension=1, tiled=True
    )
    left_f = jnp.einsum("bra,bad->brd", f_ii, amplitudes, preferred_element_type=jnp.float32).astype(
        jnp.bfloat16
    )
    left_s = jnp.einsum("bra,bad->brd", s_ii, amplitudes, preferred_element_type=jnp.float32).astype(
        jnp.bfloat16
    )
    summed = summed + jnp.einsum("brd,bdj->brj", left_f, s_jj, preferred_element_type=jnp.float32)
    summed = summed + jnp.einsum("brd,bdj->brj", left_s, f_jj, preferred_element_type=jnp.float32)
    summed = summed - energy_sum[:, None, None] * jnp.einsum(
        "brd,bdj->brj", left_s, s_jj, preferred_element_type=jnp.float32
    )

    pao_energy = jnp.diagonal(pao_fock).astype(jnp.float32)
    denom = (
        pao_energy[rows_dom][:, :, None] + pao_energy[dom_j][:, None, :] - energy_sum[:, None, None]
    )
    amp_rows = lax.dynamic_slice_in_dim(amplitudes, row_first, half_rows, 1)
    return couple_and_update(
        every_amp, global_slot, flipped, coupling_fock_element, s_ip, s_qj, summed, denom, amp_rows
    )


def solution(mesh):
    placed = (
        P("aux", ("groups", "orb"), None, None),
        P(("groups", "orb"), None, None),
        P("groups", None),
        P("groups", None),
        P("groups", None),
        P("groups", None),
        P("groups"),
        P(("groups", "orb"), None),
        P(("groups", "orb"), None),
        P(("groups", "orb"), None),
        P(("groups", "orb"), None),
    )
    return jax.shard_map(
        shards,
        mesh=mesh,
        in_specs=placed,
        out_specs=(P(("groups", "orb"), "aux", None), P(("groups", "orb"), "aux", None)),
        check_vma=False,
    )
```

```python
import functools

import jax
import jax.numpy as jnp
from jax import lax
from jax.experimental import pallas as pl
from jax.experimental.pallas import tpu as pltpu
from jax.sharding import PartitionSpec as P


def one_hot(ids, width):
    return (ids[..., None] == jnp.arange(width, dtype=ids.dtype)).astype(jnp.bfloat16)


def sel_rows(onehot, matrix):
    return jnp.einsum(
        "...rk,kc->...rc", onehot, matrix, preferred_element_type=jnp.float32
    ).astype(jnp.bfloat16)


def coupling_kernel(group, slot_ref, flip_ref, fock_ref, *refs):
    blk_refs = refs[:group]
    sip_ref, sqj_ref, own_ref, den_ref, amp_ref, res_ref, upd_ref, reach = refs[group:]
    b, step = pl.program_id(0), pl.program_id(1)
    steps = pl.num_programs(1)

    @pl.when(step == 0)
    def _():
        res_ref[...] = own_ref[...]

    total = res_ref[...]
    for k in range(group):
        at = (b * steps + step) * group + k

        @pl.when(flip_ref[at] == 1)
        def _():
            reach[...] = lax.dot_general(
                sip_ref[k], blk_refs[k][...], (((1,), (1,)), ((), ())), preferred_element_type=jnp.float32
            ).astype(jnp.bfloat16)

        @pl.when(flip_ref[at] != 1)
        def _():
            reach[...] = jnp.dot(sip_ref[k], blk_refs[k][...], preferred_element_type=jnp.float32).astype(
                jnp.bfloat16
            )

        total = total - fock_ref[at] * jnp.dot(reach[...], sqj_ref[k], preferred_element_type=jnp.float32)
    res_ref[...] = total

    @pl.when(step == steps - 1)
    def _():
        upd_ref[...] = (amp_ref[...].astype(jnp.float32) - total / den_ref[...]).astype(jnp.bfloat16)


def couple_and_update(every_amp, global_slot, flipped, fock, s_ip, s_qj, own, denom, amp_rows, group=4):
    slots, couplings = global_slot.shape
    group = group if couplings % group == 0 else 1
    steps = couplings // group
    rows, cols = own.shape[1], own.shape[2]
    extent = every_amp.shape[1]

    def block_spec(k):
        return pl.BlockSpec(
            (None, extent, extent), lambda b, t, gs, fl, fe: (gs[(b * steps + t) * group + k], 0, 0)
        )

    per_slot = lambda b, t, gs, fl, fe: (b, 0, 0)
    grid_spec = pltpu.PrefetchScalarGridSpec(
        num_scalar_prefetch=3,
        grid=(slots, steps),
        in_specs=[block_spec(k) for k in range(group)]
        + [
            pl.BlockSpec((None, group, rows, extent), lambda b, t, gs, fl, fe: (b, t, 0, 0)),
            pl.BlockSpec((None, group, extent, cols), lambda b, t, gs, fl, fe: (b, t, 0, 0)),
            pl.BlockSpec((None, rows, cols), per_slot),
            pl.BlockSpec((None, rows, cols), per_slot),
            pl.BlockSpec((None, rows, cols), per_slot),
        ],
        out_specs=[
            pl.BlockSpec((None, rows, cols), per_slot),
            pl.BlockSpec((None, rows, cols), per_slot),
        ],
        scratch_shapes=[pltpu.VMEM((rows, extent), jnp.bfloat16)],
    )
    flops = 4 * slots * couplings * rows * extent * extent
    moved = slots * couplings * (extent * extent * 2 + rows * extent * 2 + extent * cols * 2) + slots * rows * cols * 18
    return pl.pallas_call(
        functools.partial(coupling_kernel, group),
        grid_spec=grid_spec,
        out_shape=[
            jax.ShapeDtypeStruct(own.shape, jnp.float32),
            jax.ShapeDtypeStruct(own.shape, jnp.bfloat16),
        ],
        compiler_params=pltpu.CompilerParams(dimension_semantics=("arbitrary", "arbitrary")),
        cost_estimate=pl.CostEstimate(flops=flops, bytes_accessed=moved, transcendentals=0),
    )(
        global_slot.reshape(-1),
        flipped.astype(jnp.int32).reshape(-1),
        fock.reshape(-1),
        *([every_amp] * group),
        s_ip,
        s_qj,
        own,
        denom,
        amp_rows,
    )


def shards(
    exchange_integral_halves,
    amplitudes,
    pair_slot_orbitals,
    pao_domain,
    pao_intersection,
    pao_fock,
    occ_energy,
    coupled_pair_owner,
    coupled_pair_slot,
    coupling_swap_flag,
    coupling_fock_element,
):
    slot_count, extent = amplitudes.shape[0], amplitudes.shape[1]
    paos = pao_intersection.shape[0]
    halves = lax.axis_size("aux")
    owner_index = lax.axis_index("orb")
    aux_index = lax.axis_index("aux")
    half_rows = extent // halves
    row_first = aux_index * half_rows

    every_amp = lax.all_gather(amplitudes, "orb", axis=0, tiled=True)

    own_slots = owner_index * slot_count + jnp.arange(slot_count, dtype=jnp.int32)
    orb_i = pair_slot_orbitals[own_slots, 0]
    orb_j = pair_slot_orbitals[own_slots, 1]
    dom_i = pao_domain[orb_i]
    dom_j = pao_domain[orb_j]
    rows_dom = lax.dynamic_slice_in_dim(dom_i, row_first, half_rows, 1)
    energy_sum = occ_energy[orb_i] + occ_energy[orb_j]

    global_slot = coupled_pair_owner * slot_count + coupled_pair_slot
    flipped = coupling_swap_flag == 1
    first_orb = pair_slot_orbitals[global_slot, 0]
    second_orb = pair_slot_orbitals[global_slot, 1]
    orb_p = jnp.where(flipped, second_orb, first_orb)
    orb_q = jnp.where(flipped, first_orb, second_orb)

    oh_rows = one_hot(rows_dom, paos)
    oh_i = one_hot(dom_i, paos)
    oh_j = one_hot(dom_j, paos)
    oh_p = one_hot(pao_domain[orb_p], paos)
    oh_q = one_hot(pao_domain[orb_q], paos)

    rs = sel_rows(oh_rows, pao_intersection)
    rf = sel_rows(oh_rows, pao_fock)
    s_ii = jnp.einsum("brk,bak->bra", rs, oh_i, preferred_element_type=jnp.float32).astype(jnp.bfloat16)
    f_ii = jnp.einsum("brk,bak->bra", rf, oh_i, preferred_element_type=jnp.float32).astype(jnp.bfloat16)
    js = sel_rows(oh_j, pao_intersection)
    jf = sel_rows(oh_j, pao_fock)
    s_jj = jnp.einsum("bjk,bak->bja", js, oh_j, preferred_element_type=jnp.float32).astype(jnp.bfloat16)
    f_jj = jnp.einsum("bjk,bak->bja", jf, oh_j, preferred_element_type=jnp.float32).astype(jnp.bfloat16)
    col_s = jnp.einsum("kc,bjc->bkj", pao_intersection, oh_j, preferred_element_type=jnp.float32).astype(
        jnp.bfloat16
    )
    s_ip = jnp.einsum("brk,bcpk->bcrp", rs, oh_p, preferred_element_type=jnp.float32).astype(jnp.bfloat16)
    s_qj = jnp.einsum("bcqk,bkj->bcqj", oh_q, col_s, preferred_element_type=jnp.float32).astype(jnp.bfloat16)

    summed = lax.psum_scatter(
        exchange_integral_halves[0], "aux", scatter_dimension=1, tiled=True
    )
    left_f = jnp.einsum("bra,bad->brd", f_ii, amplitudes, preferred_element_type=jnp.float32).astype(
        jnp.bfloat16
    )
    left_s = jnp.einsum("bra,bad->brd", s_ii, amplitudes, preferred_element_type=jnp.float32).astype(
        jnp.bfloat16
    )
    summed = summed + jnp.einsum("brd,bdj->brj", left_f, s_jj, preferred_element_type=jnp.float32)
    summed = summed + jnp.einsum("brd,bdj->brj", left_s, f_jj, preferred_element_type=jnp.float32)
    summed = summed - energy_sum[:, None, None] * jnp.einsum(
        "brd,bdj->brj", left_s, s_jj, preferred_element_type=jnp.float32
    )

    pao_energy = jnp.diagonal(pao_fock).astype(jnp.float32)
    denom = (
        pao_energy[rows_dom][:, :, None] + pao_energy[dom_j][:, None, :] - energy_sum[:, None, None]
    )
    amp_rows = lax.dynamic_slice_in_dim(amplitudes, row_first, half_rows, 1)
    return couple_and_update(
        every_amp, global_slot, flipped, coupling_fock_element, s_ip, s_qj, summed, denom, amp_rows
    )


def solution(mesh):
    placed = (
        P("aux", ("groups", "orb"), None, None),
        P(("groups", "orb"), None, None),
        P("groups", None),
        P("groups", None),
        P("groups", None),
        P("groups", None),
        P("groups"),
        P(("groups", "orb"), None),
        P(("groups", "orb"), None),
        P(("groups", "orb"), None),
        P(("groups", "orb"), None),
    )
    return jax.shard_map(
        shards,
        mesh=mesh,
        in_specs=placed,
        out_specs=(P(("groups", "orb"), "aux", None), P(("groups", "orb"), "aux", None)),
        check_vma=False,
    )
```

```python
import functools

import jax
import jax.numpy as jnp
from jax import lax
from jax.experimental import pallas as pl
from jax.experimental.pallas import tpu as pltpu
from jax.sharding import PartitionSpec as P


def one_hot(ids, width):
    return (ids[..., None] == jnp.arange(width, dtype=ids.dtype)).astype(jnp.bfloat16)


def sel_rows(onehot, matrix):
    return jnp.einsum(
        "...rk,kc->...rc", onehot, matrix, preferred_element_type=jnp.float32
    ).astype(jnp.bfloat16)


def coupling_kernel(group, slot_ref, flip_ref, fock_ref, *refs):
    blk_refs = refs[:group]
    sip_ref, sqj_ref, own_ref, den_ref, amp_ref, res_ref, upd_ref, reach = refs[group:]
    b, step = pl.program_id(0), pl.program_id(1)
    steps = pl.num_programs(1)

    @pl.when(step == 0)
    def _():
        res_ref[...] = own_ref[...]

    total = res_ref[...]
    for k in range(group):
        at = (b * steps + step) * group + k
        block = blk_refs[k][...]
        block = jnp.where(flip_ref[at] == 1, block.T, block)
        reach = jnp.dot(sip_ref[k], block, preferred_element_type=jnp.float32).astype(jnp.bfloat16)
        total = total - fock_ref[at] * jnp.dot(reach, sqj_ref[k], preferred_element_type=jnp.float32)
    res_ref[...] = total

    @pl.when(step == steps - 1)
    def _():
        upd_ref[...] = (amp_ref[...].astype(jnp.float32) - total / den_ref[...]).astype(jnp.bfloat16)


def couple_and_update(every_amp, global_slot, flipped, fock, s_ip, s_qj, own, denom, amp_rows, group=8):
    slots, couplings = global_slot.shape
    group = group if couplings % group == 0 else 1
    steps = couplings // group
    rows, cols = own.shape[1], own.shape[2]
    extent = every_amp.shape[1]

    def block_spec(k):
        return pl.BlockSpec(
            (None, extent, extent), lambda b, t, gs, fl, fe: (gs[(b * steps + t) * group + k], 0, 0)
        )

    per_slot = lambda b, t, gs, fl, fe: (b, 0, 0)
    grid_spec = pltpu.PrefetchScalarGridSpec(
        num_scalar_prefetch=3,
        grid=(slots, steps),
        in_specs=[block_spec(k) for k in range(group)]
        + [
            pl.BlockSpec((None, group, rows, extent), lambda b, t, gs, fl, fe: (b, t, 0, 0)),
            pl.BlockSpec((None, group, extent, cols), lambda b, t, gs, fl, fe: (b, t, 0, 0)),
            pl.BlockSpec((None, rows, cols), per_slot),
            pl.BlockSpec((None, rows, cols), per_slot),
            pl.BlockSpec((None, rows, cols), per_slot),
        ],
        out_specs=[
            pl.BlockSpec((None, rows, cols), per_slot),
            pl.BlockSpec((None, rows, cols), per_slot),
        ],
        scratch_shapes=[pltpu.VMEM((rows, extent), jnp.bfloat16)],
    )
    flops = 4 * slots * couplings * rows * extent * extent
    moved = slots * couplings * (extent * extent * 2 + rows * extent * 2 + extent * cols * 2) + slots * rows * cols * 18
    return pl.pallas_call(
        functools.partial(coupling_kernel, group),
        grid_spec=grid_spec,
        out_shape=[
            jax.ShapeDtypeStruct(own.shape, jnp.float32),
            jax.ShapeDtypeStruct(own.shape, jnp.bfloat16),
        ],
        compiler_params=pltpu.CompilerParams(dimension_semantics=("arbitrary", "arbitrary")),
        cost_estimate=pl.CostEstimate(flops=flops, bytes_accessed=moved, transcendentals=0),
    )(
        global_slot.reshape(-1),
        flipped.astype(jnp.int32).reshape(-1),
        fock.reshape(-1),
        *([every_amp] * group),
        s_ip,
        s_qj,
        own,
        denom,
        amp_rows,
    )


def shards(
    exchange_integral_halves,
    amplitudes,
    pair_slot_orbitals,
    pao_domain,
    pao_intersection,
    pao_fock,
    occ_energy,
    coupled_pair_owner,
    coupled_pair_slot,
    coupling_swap_flag,
    coupling_fock_element,
):
    slot_count, extent = amplitudes.shape[0], amplitudes.shape[1]
    paos = pao_intersection.shape[0]
    halves = lax.axis_size("aux")
    owner_index = lax.axis_index("orb")
    aux_index = lax.axis_index("aux")
    half_rows = extent // halves
    row_first = aux_index * half_rows

    every_amp = lax.all_gather(amplitudes, "orb", axis=0, tiled=True)

    own_slots = owner_index * slot_count + jnp.arange(slot_count, dtype=jnp.int32)
    orb_i = pair_slot_orbitals[own_slots, 0]
    orb_j = pair_slot_orbitals[own_slots, 1]
    dom_i = pao_domain[orb_i]
    dom_j = pao_domain[orb_j]
    rows_dom = lax.dynamic_slice_in_dim(dom_i, row_first, half_rows, 1)
    energy_sum = occ_energy[orb_i] + occ_energy[orb_j]

    global_slot = coupled_pair_owner * slot_count + coupled_pair_slot
    flipped = coupling_swap_flag == 1
    first_orb = pair_slot_orbitals[global_slot, 0]
    second_orb = pair_slot_orbitals[global_slot, 1]
    orb_p = jnp.where(flipped, second_orb, first_orb)
    orb_q = jnp.where(flipped, first_orb, second_orb)

    oh_rows = one_hot(rows_dom, paos)
    oh_i = one_hot(dom_i, paos)
    oh_j = one_hot(dom_j, paos)
    oh_p = one_hot(pao_domain[orb_p], paos)
    oh_q = one_hot(pao_domain[orb_q], paos)

    rs = sel_rows(oh_rows, pao_intersection)
    rf = sel_rows(oh_rows, pao_fock)
    s_ii = jnp.einsum("brk,bak->bra", rs, oh_i, preferred_element_type=jnp.float32).astype(jnp.bfloat16)
    f_ii = jnp.einsum("brk,bak->bra", rf, oh_i, preferred_element_type=jnp.float32).astype(jnp.bfloat16)
    js = sel_rows(oh_j, pao_intersection)
    jf = sel_rows(oh_j, pao_fock)
    s_jj = jnp.einsum("bjk,bak->bja", js, oh_j, preferred_element_type=jnp.float32).astype(jnp.bfloat16)
    f_jj = jnp.einsum("bjk,bak->bja", jf, oh_j, preferred_element_type=jnp.float32).astype(jnp.bfloat16)
    col_s = jnp.einsum("kc,bjc->bkj", pao_intersection, oh_j, preferred_element_type=jnp.float32).astype(
        jnp.bfloat16
    )
    s_ip = jnp.einsum("brk,bcpk->bcrp", rs, oh_p, preferred_element_type=jnp.float32).astype(jnp.bfloat16)
    s_qj = jnp.einsum("bcqk,bkj->bcqj", oh_q, col_s, preferred_element_type=jnp.float32).astype(jnp.bfloat16)

    summed = lax.psum_scatter(
        exchange_integral_halves[0], "aux", scatter_dimension=1, tiled=True
    )
    left_f = jnp.einsum("bra,bad->brd", f_ii, amplitudes, preferred_element_type=jnp.float32).astype(
        jnp.bfloat16
    )
    left_s = jnp.einsum("bra,bad->brd", s_ii, amplitudes, preferred_element_type=jnp.float32).astype(
        jnp.bfloat16
    )
    summed = summed + jnp.einsum("brd,bdj->brj", left_f, s_jj, preferred_element_type=jnp.float32)
    summed = summed + jnp.einsum("brd,bdj->brj", left_s, f_jj, preferred_element_type=jnp.float32)
    summed = summed - energy_sum[:, None, None] * jnp.einsum(
        "brd,bdj->brj", left_s, s_jj, preferred_element_type=jnp.float32
    )

    pao_energy = jnp.diagonal(pao_fock).astype(jnp.float32)
    denom = (
        pao_energy[rows_dom][:, :, None] + pao_energy[dom_j][:, None, :] - energy_sum[:, None, None]
    )
    amp_rows = lax.dynamic_slice_in_dim(amplitudes, row_first, half_rows, 1)
    return couple_and_update(
        every_amp, global_slot, flipped, coupling_fock_element, s_ip, s_qj, summed, denom, amp_rows
    )


def solution(mesh):
    placed = (
        P("aux", ("groups", "orb"), None, None),
        P(("groups", "orb"), None, None),
        P("groups", None),
        P("groups", None),
        P("groups", None),
        P("groups", None),
        P("groups"),
        P(("groups", "orb"), None),
        P(("groups", "orb"), None),
        P(("groups", "orb"), None),
        P(("groups", "orb"), None),
    )
    return jax.shard_map(
        shards,
        mesh=mesh,
        in_specs=placed,
        out_specs=(P(("groups", "orb"), "aux", None), P(("groups", "orb"), "aux", None)),
        check_vma=False,
    )
```

```python
import functools

import jax
import jax.numpy as jnp
from jax import lax
from jax.experimental import pallas as pl
from jax.experimental.pallas import tpu as pltpu
from jax.sharding import PartitionSpec as P


def one_hot(ids, width):
    return (ids[..., None] == jnp.arange(width, dtype=ids.dtype)).astype(jnp.bfloat16)


def sel_rows(onehot, matrix):
    return jnp.einsum(
        "...rk,kc->...rc", onehot, matrix, preferred_element_type=jnp.float32
    ).astype(jnp.bfloat16)


def coupling_kernel(group, slot_ref, flip_ref, fock_ref, esum_ref, *refs):
    blk_refs = refs[:group]
    both_ref, own_ref, erow_ref, ecol_ref, amp_ref, res_ref, upd_ref = refs[group:]
    rows = own_ref.shape[0]
    b, step = pl.program_id(0), pl.program_id(1)
    steps = pl.num_programs(1)

    @pl.when(step == 0)
    def _():
        res_ref[...] = own_ref[...]

    total = res_ref[...]
    for k in range(group):
        at = (b * steps + step) * group + k
        block = blk_refs[k][...]
        block = jnp.where(flip_ref[at] == 1, block.T, block)
        reach = jnp.dot(both_ref[k, :rows], block, preferred_element_type=jnp.float32).astype(jnp.bfloat16)
        total = total - fock_ref[at] * jnp.dot(reach, both_ref[k, rows:], preferred_element_type=jnp.float32)
    res_ref[...] = total

    @pl.when(step == steps - 1)
    def _():
        denom = erow_ref[...] + ecol_ref[...] - esum_ref[b]
        upd_ref[...] = (amp_ref[...].astype(jnp.float32) - total / denom).astype(jnp.bfloat16)


def couple_and_update(
    every_amp, global_slot, flipped, fock, s_ip, s_qj, own, e_rows, e_cols, energy_sum, amp_rows, group=8
):
    slots, couplings = global_slot.shape
    group = group if couplings % group == 0 else 1
    steps = couplings // group
    rows, cols = own.shape[1], own.shape[2]
    extent = every_amp.shape[1]

    def block_spec(k):
        return pl.BlockSpec(
            (None, extent, extent), lambda b, t, gs, fl, fe, es: (gs[(b * steps + t) * group + k], 0, 0)
        )

    per_slot = lambda b, t, gs, fl, fe, es: (b, 0, 0)
    grid_spec = pltpu.PrefetchScalarGridSpec(
        num_scalar_prefetch=4,
        grid=(slots, steps),
        in_specs=[block_spec(k) for k in range(group)]
        + [
            pl.BlockSpec((None, group, rows + extent, extent), lambda b, t, gs, fl, fe, es: (b, t, 0, 0)),
            pl.BlockSpec((None, rows, cols), per_slot),
            pl.BlockSpec((None, rows, 1), per_slot),
            pl.BlockSpec((None, 1, cols), per_slot),
            pl.BlockSpec((None, rows, cols), per_slot),
        ],
        out_specs=[
            pl.BlockSpec((None, rows, cols), per_slot),
            pl.BlockSpec((None, rows, cols), per_slot),
        ],
    )
    flops = 4 * slots * couplings * rows * extent * extent
    moved = slots * couplings * (extent * extent * 2 + rows * extent * 2 + extent * cols * 2) + slots * rows * cols * 18
    return pl.pallas_call(
        functools.partial(coupling_kernel, group),
        grid_spec=grid_spec,
        out_shape=[
            jax.ShapeDtypeStruct(own.shape, jnp.float32),
            jax.ShapeDtypeStruct(own.shape, jnp.bfloat16),
        ],
        compiler_params=pltpu.CompilerParams(dimension_semantics=("arbitrary", "arbitrary")),
        cost_estimate=pl.CostEstimate(flops=flops, bytes_accessed=moved, transcendentals=0),
    )(
        global_slot.reshape(-1),
        flipped.astype(jnp.int32).reshape(-1),
        fock.reshape(-1),
        energy_sum,
        *([every_amp] * group),
        jnp.concatenate([s_ip, s_qj], axis=2),
        own,
        e_rows[:, :, None],
        e_cols[:, None, :],
        amp_rows,
    )


def shards(
    exchange_integral_halves,
    amplitudes,
    pair_slot_orbitals,
    pao_domain,
    pao_intersection,
    pao_fock,
    occ_energy,
    coupled_pair_owner,
    coupled_pair_slot,
    coupling_swap_flag,
    coupling_fock_element,
):
    slot_count, extent = amplitudes.shape[0], amplitudes.shape[1]
    paos = pao_intersection.shape[0]
    halves = lax.axis_size("aux")
    owner_index = lax.axis_index("orb")
    aux_index = lax.axis_index("aux")
    half_rows = extent // halves
    row_first = aux_index * half_rows

    every_amp = lax.all_gather(amplitudes, "orb", axis=0, tiled=True)

    own_slots = owner_index * slot_count + jnp.arange(slot_count, dtype=jnp.int32)
    orb_i = pair_slot_orbitals[own_slots, 0]
    orb_j = pair_slot_orbitals[own_slots, 1]
    dom_i = pao_domain[orb_i]
    dom_j = pao_domain[orb_j]
    rows_dom = lax.dynamic_slice_in_dim(dom_i, row_first, half_rows, 1)
    energy_sum = occ_energy[orb_i] + occ_energy[orb_j]

    global_slot = coupled_pair_owner * slot_count + coupled_pair_slot
    flipped = coupling_swap_flag == 1
    first_orb = pair_slot_orbitals[global_slot, 0]
    second_orb = pair_slot_orbitals[global_slot, 1]
    orb_p = jnp.where(flipped, second_orb, first_orb)
    orb_q = jnp.where(flipped, first_orb, second_orb)

    oh_rows = one_hot(rows_dom, paos)
    oh_i = one_hot(dom_i, paos)
    oh_j = one_hot(dom_j, paos)
    oh_p = one_hot(pao_domain[orb_p], paos)
    oh_q = one_hot(pao_domain[orb_q], paos)

    rs = sel_rows(oh_rows, pao_intersection)
    rf = sel_rows(oh_rows, pao_fock)
    s_ii = jnp.einsum("brk,bak->bra", rs, oh_i, preferred_element_type=jnp.float32).astype(jnp.bfloat16)
    f_ii = jnp.einsum("brk,bak->bra", rf, oh_i, preferred_element_type=jnp.float32).astype(jnp.bfloat16)
    js = sel_rows(oh_j, pao_intersection)
    jf = sel_rows(oh_j, pao_fock)
    s_jj = jnp.einsum("bjk,bak->bja", js, oh_j, preferred_element_type=jnp.float32).astype(jnp.bfloat16)
    f_jj = jnp.einsum("bjk,bak->bja", jf, oh_j, preferred_element_type=jnp.float32).astype(jnp.bfloat16)
    col_s = jnp.einsum("kc,bjc->bkj", pao_intersection, oh_j, preferred_element_type=jnp.float32).astype(
        jnp.bfloat16
    )
    s_ip = jnp.einsum("brk,bcpk->bcrp", rs, oh_p, preferred_element_type=jnp.float32).astype(jnp.bfloat16)
    s_qj = jnp.einsum("bcqk,bkj->bcqj", oh_q, col_s, preferred_element_type=jnp.float32).astype(jnp.bfloat16)

    summed = lax.psum_scatter(
        exchange_integral_halves[0], "aux", scatter_dimension=1, tiled=True
    )
    left_f = jnp.einsum("bra,bad->brd", f_ii, amplitudes, preferred_element_type=jnp.float32).astype(
        jnp.bfloat16
    )
    left_s = jnp.einsum("bra,bad->brd", s_ii, amplitudes, preferred_element_type=jnp.float32).astype(
        jnp.bfloat16
    )
    summed = summed + jnp.einsum("brd,bdj->brj", left_f, s_jj, preferred_element_type=jnp.float32)
    summed = summed + jnp.einsum("brd,bdj->brj", left_s, f_jj, preferred_element_type=jnp.float32)
    summed = summed - energy_sum[:, None, None] * jnp.einsum(
        "brd,bdj->brj", left_s, s_jj, preferred_element_type=jnp.float32
    )

    pao_energy = jnp.diagonal(pao_fock).astype(jnp.float32)
    amp_rows = lax.dynamic_slice_in_dim(amplitudes, row_first, half_rows, 1)
    return couple_and_update(
        every_amp,
        global_slot,
        flipped,
        coupling_fock_element,
        s_ip,
        s_qj,
        summed,
        pao_energy[rows_dom],
        pao_energy[dom_j],
        energy_sum,
        amp_rows,
    )


def solution(mesh):
    placed = (
        P("aux", ("groups", "orb"), None, None),
        P(("groups", "orb"), None, None),
        P("groups", None),
        P("groups", None),
        P("groups", None),
        P("groups", None),
        P("groups"),
        P(("groups", "orb"), None),
        P(("groups", "orb"), None),
        P(("groups", "orb"), None),
        P(("groups", "orb"), None),
    )
    return jax.shard_map(
        shards,
        mesh=mesh,
        in_specs=placed,
        out_specs=(P(("groups", "orb"), "aux", None), P(("groups", "orb"), "aux", None)),
        check_vma=False,
    )
```

```python
import functools

import jax
import jax.numpy as jnp
from jax import lax
from jax.experimental import pallas as pl
from jax.experimental.pallas import tpu as pltpu
from jax.sharding import PartitionSpec as P


def one_hot(ids, width):
    return (ids[..., None] == jnp.arange(width, dtype=ids.dtype)).astype(jnp.bfloat16)


def sel_rows(onehot, matrix):
    return jnp.einsum(
        "...rk,kc->...rc", onehot, matrix, preferred_element_type=jnp.float32
    ).astype(jnp.bfloat16)


def coupling_kernel(group, slot_ref, last_ref, pick_ref, flip_ref, fock_ref, *refs):
    blk_refs = refs[:group]
    tail_refs = refs[group:2 * group]
    sip_ref, sqj_ref, own_ref, den_ref, amp_ref, res_ref, upd_ref, reach = refs[2 * group:]
    b, step = pl.program_id(0), pl.program_id(1)
    steps = pl.num_programs(1)

    @pl.when(step == 0)
    def _():
        res_ref[...] = own_ref[...]

    total = res_ref[...]
    for k in range(group):
        at = (b * steps + step) * group + k
        block = jnp.where(pick_ref[at] == 1, tail_refs[k][...], blk_refs[k][...])
        block = jnp.where(flip_ref[at] == 1, block.T, block)
        reach = jnp.dot(sip_ref[k], block, preferred_element_type=jnp.float32).astype(jnp.bfloat16)
        total = total - fock_ref[at] * jnp.dot(reach, sqj_ref[k], preferred_element_type=jnp.float32)
    res_ref[...] = total

    @pl.when(step == steps - 1)
    def _():
        upd_ref[...] = (amp_ref[...].astype(jnp.float32) - total / den_ref[...]).astype(jnp.bfloat16)


def couple_and_update(
    head_amp, tail_amp, head_slot, tail_slot, pick, flipped, fock, s_ip, s_qj, own, denom, amp_rows, group=8
):
    slots, couplings = head_slot.shape
    group = group if couplings % group == 0 else 1
    steps = couplings // group
    rows, cols = own.shape[1], own.shape[2]
    extent = head_amp.shape[1]

    def block_spec(k):
        return pl.BlockSpec(
            (None, extent, extent), lambda b, t, gs, ls, pk, fl, fe: (gs[(b * steps + t) * group + k], 0, 0)
        )

    def tail_spec(k):
        return pl.BlockSpec(
            (None, extent, extent), lambda b, t, gs, ls, pk, fl, fe: (ls[(b * steps + t) * group + k], 0, 0)
        )

    per_slot = lambda b, t, gs, ls, pk, fl, fe: (b, 0, 0)
    grid_spec = pltpu.PrefetchScalarGridSpec(
        num_scalar_prefetch=5,
        grid=(slots, steps),
        in_specs=[block_spec(k) for k in range(group)]
        + [tail_spec(k) for k in range(group)]
        + [
            pl.BlockSpec((None, group, rows, extent), lambda b, t, gs, ls, pk, fl, fe: (b, t, 0, 0)),
            pl.BlockSpec((None, group, extent, cols), lambda b, t, gs, ls, pk, fl, fe: (b, t, 0, 0)),
            pl.BlockSpec((None, rows, cols), per_slot),
            pl.BlockSpec((None, rows, cols), per_slot),
            pl.BlockSpec((None, rows, cols), per_slot),
        ],
        out_specs=[
            pl.BlockSpec((None, rows, cols), per_slot),
            pl.BlockSpec((None, rows, cols), per_slot),
        ],
        scratch_shapes=[pltpu.VMEM((rows, extent), jnp.bfloat16)],
    )
    flops = 4 * slots * couplings * rows * extent * extent
    moved = slots * couplings * (extent * extent * 2 + rows * extent * 2 + extent * cols * 2) + slots * rows * cols * 18
    return pl.pallas_call(
        functools.partial(coupling_kernel, group),
        grid_spec=grid_spec,
        out_shape=[
            jax.ShapeDtypeStruct(own.shape, jnp.float32),
            jax.ShapeDtypeStruct(own.shape, jnp.bfloat16),
        ],
        compiler_params=pltpu.CompilerParams(dimension_semantics=("arbitrary", "arbitrary")),
        cost_estimate=pl.CostEstimate(flops=flops, bytes_accessed=moved, transcendentals=0),
    )(
        head_slot.reshape(-1),
        tail_slot.reshape(-1),
        pick.astype(jnp.int32).reshape(-1),
        flipped.astype(jnp.int32).reshape(-1),
        fock.reshape(-1),
        *([head_amp] * group),
        *([tail_amp] * group),
        s_ip,
        s_qj,
        own,
        denom,
        amp_rows,
    )


def shards(
    exchange_integral_halves,
    amplitudes,
    pair_slot_orbitals,
    pao_domain,
    pao_intersection,
    pao_fock,
    occ_energy,
    coupled_pair_owner,
    coupled_pair_slot,
    coupling_swap_flag,
    coupling_fock_element,
):
    slot_count, extent = amplitudes.shape[0], amplitudes.shape[1]
    paos = pao_intersection.shape[0]
    halves = lax.axis_size("aux")
    owner_index = lax.axis_index("orb")
    aux_index = lax.axis_index("aux")
    half_rows = extent // halves
    row_first = aux_index * half_rows

    owners = lax.axis_size("orb")
    head_amp = lax.all_gather(amplitudes[: slot_count - 1], "orb", axis=0, tiled=True)
    tail_amp = lax.all_to_all(
        jnp.broadcast_to(amplitudes[slot_count - 1], (owners, extent, extent)), "orb", 0, 0, tiled=True
    )

    own_slots = owner_index * slot_count + jnp.arange(slot_count, dtype=jnp.int32)
    orb_i = pair_slot_orbitals[own_slots, 0]
    orb_j = pair_slot_orbitals[own_slots, 1]
    dom_i = pao_domain[orb_i]
    dom_j = pao_domain[orb_j]
    rows_dom = lax.dynamic_slice_in_dim(dom_i, row_first, half_rows, 1)
    energy_sum = occ_energy[orb_i] + occ_energy[orb_j]

    global_slot = coupled_pair_owner * slot_count + coupled_pair_slot
    flipped = coupling_swap_flag == 1
    first_orb = pair_slot_orbitals[global_slot, 0]
    second_orb = pair_slot_orbitals[global_slot, 1]
    orb_p = jnp.where(flipped, second_orb, first_orb)
    orb_q = jnp.where(flipped, first_orb, second_orb)

    oh_rows = one_hot(rows_dom, paos)
    oh_i = one_hot(dom_i, paos)
    oh_j = one_hot(dom_j, paos)
    oh_p = one_hot(pao_domain[orb_p], paos)
    oh_q = one_hot(pao_domain[orb_q], paos)

    rs = sel_rows(oh_rows, pao_intersection)
    rf = sel_rows(oh_rows, pao_fock)
    s_ii = jnp.einsum("brk,bak->bra", rs, oh_i, preferred_element_type=jnp.float32).astype(jnp.bfloat16)
    f_ii = jnp.einsum("brk,bak->bra", rf, oh_i, preferred_element_type=jnp.float32).astype(jnp.bfloat16)
    js = sel_rows(oh_j, pao_intersection)
    jf = sel_rows(oh_j, pao_fock)
    s_jj = jnp.einsum("bjk,bak->bja", js, oh_j, preferred_element_type=jnp.float32).astype(jnp.bfloat16)
    f_jj = jnp.einsum("bjk,bak->bja", jf, oh_j, preferred_element_type=jnp.float32).astype(jnp.bfloat16)
    col_s = jnp.einsum("kc,bjc->bkj", pao_intersection, oh_j, preferred_element_type=jnp.float32).astype(
        jnp.bfloat16
    )
    s_ip = jnp.einsum("brk,bcpk->bcrp", rs, oh_p, preferred_element_type=jnp.float32).astype(jnp.bfloat16)
    s_qj = jnp.einsum("bcqk,bkj->bcqj", oh_q, col_s, preferred_element_type=jnp.float32).astype(jnp.bfloat16)

    summed = lax.psum_scatter(
        exchange_integral_halves[0], "aux", scatter_dimension=1, tiled=True
    )
    left_f = jnp.einsum("bra,bad->brd", f_ii, amplitudes, preferred_element_type=jnp.float32).astype(
        jnp.bfloat16
    )
    left_s = jnp.einsum("bra,bad->brd", s_ii, amplitudes, preferred_element_type=jnp.float32).astype(
        jnp.bfloat16
    )
    summed = summed + jnp.einsum("brd,bdj->brj", left_f, s_jj, preferred_element_type=jnp.float32)
    summed = summed + jnp.einsum("brd,bdj->brj", left_s, f_jj, preferred_element_type=jnp.float32)
    summed = summed - energy_sum[:, None, None] * jnp.einsum(
        "brd,bdj->brj", left_s, s_jj, preferred_element_type=jnp.float32
    )

    pao_energy = jnp.diagonal(pao_fock).astype(jnp.float32)
    denom = (
        pao_energy[rows_dom][:, :, None] + pao_energy[dom_j][:, None, :] - energy_sum[:, None, None]
    )
    amp_rows = lax.dynamic_slice_in_dim(amplitudes, row_first, half_rows, 1)
    pick = coupled_pair_slot == slot_count - 1
    head_slot = coupled_pair_owner * (slot_count - 1) + jnp.minimum(coupled_pair_slot, slot_count - 2)
    return couple_and_update(
        head_amp,
        tail_amp,
        head_slot,
        coupled_pair_owner,
        pick,
        flipped,
        coupling_fock_element,
        s_ip,
        s_qj,
        summed,
        denom,
        amp_rows,
    )


def solution(mesh):
    placed = (
        P("aux", ("groups", "orb"), None, None),
        P(("groups", "orb"), None, None),
        P("groups", None),
        P("groups", None),
        P("groups", None),
        P("groups", None),
        P("groups"),
        P(("groups", "orb"), None),
        P(("groups", "orb"), None),
        P(("groups", "orb"), None),
        P(("groups", "orb"), None),
    )
    return jax.shard_map(
        shards,
        mesh=mesh,
        in_specs=placed,
        out_specs=(P(("groups", "orb"), "aux", None), P(("groups", "orb"), "aux", None)),
        check_vma=False,
    )
```
